256 devices in a mesh: fsdp: 32 (over x, z), expert: 8 (over y, core).
Axes of the slice: x: 4, y: 4, z: 8, core: 2. Of those that a mesh axis runs over, the one named last changes fastest.
Arguments:
- expert_rows: bfloat16 [32, 128, 8, 10, 2880], P('fsdp', 'expert'), may hold values from -6 to 6
- residual: bfloat16 [32768, 2880], P(('fsdp', 'expert')), may hold values from -3 to 3
- route_ids: int32 [32768, 4], P(('fsdp', 'expert')), may hold values from 0 to 127, as said below
- route_weights: float32 [32768, 4], P(('fsdp', 'expert')), may hold values from 0.05 to 1
- route_slots: int32 [32768, 4], P(('fsdp', 'expert')), may hold values from 0 to 9, as said below
- doc_start: int32 [32768], P('fsdp'), may hold values from 0 to 32767, as said below
- norm_gain: float32 [2880], replicated, may hold values from 0.5 to 12, as said below
- projection_weight: bfloat16 [2880, 8, 640], P('fsdp', 'expert'), may hold values from -0.109375 to 0.109375
- projection_bias: float32 [8, 640], P('expert'), may hold values from -3 to 3
- sinks: float32 [8, 8], P('expert'), may hold values from -2 to 5
- output_weight: bfloat16 [8, 512, 2880], P('expert', 'fsdp'), may hold values from -0.25 to 0.25
- b_out: float32 [2880], replicated, may hold values from -3 to 3
Outputs:
- block_out: bfloat16 [32768, 2880], P(('fsdp', 'expert'))
The draws below stay inside these ranges and needn't reach their ends.
Inputs may be any that keep to these rules, and one draw needn't show every extreme that they name: `route_ids`: each token names 4 different experts. Among the tokens of each aligned block of 128 tokens (one device's), no expert is named more than 10 times, and some expert is named exactly 10 times in every block. `route_slots`: the slot of a token's route counts the earlier tokens of the same aligned block of 128 tokens that name the same expert. doc_start of a token is the position where its document begins: it never exceeds the token's position, equals it at each document's first token, and is the same for all tokens of a document. `norm_gain`: Positive.
All inputs are finite; a program needn't handle non-finite values.
Results may differ from the reference program's by a relative error of at most 0.04.
The reference program's roundings to bfloat16 on the way count: a program that leaves them out, or rounds other values in their place, can miss the bound.
Values may be sent and summed in bfloat16 or wider, within the bound.
No kernel may reach another device: no remote copies, remote signals or barrier semaphores. Data moves between devices by JAX's collectives and lax.ppermute only.
A program may use at most 128 MiB of HBM per device.

```python
import math
import jax
import jax.numpy as jnp
from jax import lax

MODEL_DIM = 2880
HEAD_SIZE = 64
KEY_HEADS = 8
QUERY_PER_KV = 8
TOPK = 4
KEYS_VISIBLE = 128
TOK_DEV = 128
EXPERTS = 128
GROUP_COLUMNS = 640
CAP = 10
SHARD_TOKENS = 1024
TOKENS = 32768
N_FSDP = 32
N_EXPERT = 8


def route_tables(key):
    base_key = jax.random.fold_in(key, 4242)
    blocks_total = TOKENS // TOK_DEV
    per_group = SHARD_TOKENS // TOK_DEV

    def one_block(block_id):
        block_key = jax.random.fold_in(base_key, block_id)
        key_order, key_hot, key_rows, key_cols, key_delta = jax.random.split(block_key, 5)
        group_key = jax.random.fold_in(jax.random.fold_in(base_key, 777777), block_id // per_group)
        shared_hot = jax.random.randint(group_key, (), 0, EXPERTS)
        expert_index = jnp.arange(EXPERTS, dtype=jnp.int32)
        scores = jax.random.randint(key_order, (EXPERTS,), 0, 1 << 20) * EXPERTS + expert_index + jnp.where(expert_index == shared_hot, 1 << 28, 0)
        ranked = jnp.argsort(-scores)
        hot_count = jax.random.randint(key_hot, (), EXPERTS // 32 + 1, 3 * EXPERTS // 32 + 2)
        remaining = TOPK * TOK_DEV - CAP * hot_count
        cold_count = EXPERTS - hot_count
        base_load = remaining // cold_count
        surplus = remaining % cold_count
        cold_rank = expert_index - hot_count
        spread = jnp.maximum(jnp.minimum(base_load - 1, CAP - base_load - 2), 0)
        deltas = jax.random.randint(key_delta, (EXPERTS,), 0, spread + 1)
        paired = cold_rank // 2
        pair_delta = deltas[jnp.clip(paired, 0, EXPERTS - 1)]
        in_pair = (cold_rank >= 0) & (paired < cold_count // 2)
        signed = jnp.where(in_pair, jnp.where(cold_rank % 2 == 0, pair_delta, -pair_delta), 0)
        loads_all = jnp.where(expert_index < hot_count, CAP, base_load + (cold_rank < surplus).astype(jnp.int32) + signed)
        load_ends = jnp.cumsum(loads_all)
        places = jnp.arange(TOPK * TOK_DEV, dtype=jnp.int32)
        rank_of = jnp.sum((load_ends[None, :] <= places[:, None]).astype(jnp.int32), axis=1)
        labels = ranked[rank_of]
        routes = labels.reshape(TOPK, TOK_DEV).T
        routes = routes[jax.random.permutation(key_rows, TOK_DEV)]
        column_keys = jax.random.randint(key_cols, (TOK_DEV, TOPK), 0, 1 << 20) * TOPK + jnp.arange(TOPK, dtype=jnp.int32)
        column_order = jnp.argsort(column_keys, axis=1)
        routes = jnp.take_along_axis(routes, column_order, axis=1)
        counted = jnp.sum((routes[:, :, None] == expert_index[None, None, :]).astype(jnp.int32), axis=1)
        earlier = jnp.cumsum(counted, axis=0) - counted
        slot_rank = jnp.take_along_axis(earlier, routes, axis=1)
        return (routes.astype(jnp.int32), slot_rank.astype(jnp.int32))
    all_routes, all_slots = jax.vmap(one_block)(jnp.arange(blocks_total, dtype=jnp.int32))
    return (all_routes.reshape(TOKENS, TOPK), all_slots.reshape(TOKENS, TOPK))


def draw_route_ids(key, part):
    return route_tables(key)[0]


def draw_route_slots(key, part):
    return route_tables(key)[1]


def draw_doc_start(key, part):
    positions = jnp.arange(TOKENS, dtype=jnp.int32)
    marks = jax.random.randint(jax.random.fold_in(key, 5151), (TOKENS,), 0, 192) == 0
    marks = marks | (positions == 0)
    return lax.cummax(jnp.where(marks, positions, 0), axis=0).astype(jnp.int32)


def draw_norm_gain(key, part):
    uniform_draw = jax.random.uniform(jax.random.fold_in(key, 6161), (MODEL_DIM,), jnp.float32)
    return (0.6 + 0.8 * uniform_draw).astype(jnp.float32)


def shard_levels(rng, extent, pieces, smallest, top_value):
    gain = 1.0
    for position, shards_of in pieces:
        draws = jax.random.uniform(jax.random.fold_in(jax.random.fold_in(rng, 6), position), (shards_of,), jnp.float32, smallest / len(pieces), top_value / len(pieces))
        gain = gain * jnp.repeat(jnp.exp(draws), extent[position] // shards_of).reshape((-1,) + (1,) * (len(extent) - 1 - position))
    return gain


def centred(stream_key, extent, scale, reach, pieces=(), held_as=jnp.bfloat16):
    result = scale * jax.random.normal(stream_key, extent, jnp.float32)
    if pieces:
        result = result * shard_levels(stream_key, extent, pieces, -0.22, 0.18)
    return jnp.clip(result, -reach, reach).astype(held_as)


def setup_inputs(seed: int = 0) -> dict:
    seeds = jax.random.split(jax.random.key(seed), 13)
    return {
        "expert_rows": centred(seeds[0], (N_FSDP, EXPERTS, N_EXPERT, CAP, MODEL_DIM), 1.0, 6.0, ((0, 32), (1, 8))),
        "residual": centred(seeds[1], (TOKENS, MODEL_DIM), 0.5, 3.0, ((0, 256),)),
        "route_ids": draw_route_ids(jax.random.fold_in(seeds[12], 71), 0),
        "route_weights": jnp.clip(jnp.exp(math.log(1.0) - 2.9957323 * jax.random.uniform(seeds[3], (TOKENS, TOPK), jnp.float32) ** shard_levels(seeds[3], (TOKENS, TOPK), ((0, 256),), -0.2, 0.2)), 0.05, 1.0),
        "route_slots": draw_route_slots(jax.random.fold_in(seeds[12], 71), 0),
        "doc_start": draw_doc_start(jax.random.fold_in(seeds[12], 71), 0),
        "norm_gain": draw_norm_gain(jax.random.fold_in(seeds[12], 71), 0),
        "projection_weight": centred(seeds[7], (MODEL_DIM, KEY_HEADS, GROUP_COLUMNS), MODEL_DIM ** -0.5, 0.109375, ((0, 32), (1, 8))),
        "projection_bias": centred(seeds[8], (KEY_HEADS, GROUP_COLUMNS), 0.5, 3.0, ((0, 8),), jnp.float32),
        "sinks": jnp.clip(-2.0 + 7.0 * jax.random.uniform(seeds[9], (KEY_HEADS, QUERY_PER_KV), jnp.float32) ** shard_levels(seeds[9], (KEY_HEADS, QUERY_PER_KV), ((0, 8),), -0.2, 0.2), -2.0, 5.0),
        "output_weight": centred(seeds[10], (KEY_HEADS, QUERY_PER_KV * HEAD_SIZE, MODEL_DIM), (QUERY_PER_KV * HEAD_SIZE) ** -0.5, 0.25, ((0, 8), (1, 32))),
        "b_out": centred(seeds[11], (MODEL_DIM,), 0.5, 3.0, (), jnp.float32),
    }


ROPE_BASE = 150000.0
EPSILON = 1e-05

def apply_rotation(values, positions):
    half_width = values.shape[-1] // 2
    steps_half = jnp.arange(half_width, dtype=jnp.float32)
    frequency = ROPE_BASE ** (-2.0 * steps_half / values.shape[-1])
    angles = positions.astype(jnp.float32)[:, None] * frequency[None, :]
    shape_out = (angles.shape[0],) + (1,) * (values.ndim - 2) + (half_width,)
    cosine = jnp.cos(angles).reshape(shape_out)
    sine_part = jnp.sin(angles).reshape(shape_out)
    front_half = values[..., :half_width]
    back_half = values[..., half_width:]
    return jnp.concatenate([front_half * cosine - back_half * sine_part, back_half * cosine + front_half * sine_part], axis=-1)

def attend(query_rows, extended, query_pos, key_pos, starts, sinks):
    keys_only = extended[..., :HEAD_SIZE].astype(jnp.float32)
    values_only = extended[..., HEAD_SIZE:].astype(jnp.float32)
    scores = jnp.einsum('qjgd,kjd->jgqk', query_rows.astype(jnp.float32), keys_only) * HEAD_SIZE ** (-0.5)
    allowed = (key_pos[None, :] <= query_pos[:, None]) & (key_pos[None, :] > query_pos[:, None] - KEYS_VISIBLE) & (key_pos[None, :] >= starts[:, None])
    masked = jnp.where(allowed[None, None], scores, -jnp.inf)
    row_peak = jnp.maximum(lax.optimization_barrier(jnp.max(masked, axis=-1)), sinks[:, :, None])
    exponent = jnp.exp(masked - row_peak[..., None])
    denominator = lax.optimization_barrier(jnp.sum(exponent, axis=-1)) + jnp.exp(sinks[:, :, None] - row_peak)
    weights_soft = (exponent / denominator[..., None]).astype(jnp.bfloat16)
    return jnp.einsum('jgqk,kjd->qjgd', weights_soft.astype(jnp.float32), values_only).astype(jnp.bfloat16)

def reference(expert_rows, residual, route_ids, route_weights, route_slots, doc_start, norm_gain, projection_weight, projection_bias, sinks, output_weight, b_out):
    ids_blocks = route_ids.reshape(N_FSDP, SHARD_TOKENS, TOPK)
    weight_blocks = route_weights.reshape(N_FSDP, SHARD_TOKENS, TOPK)
    slot_blocks = route_slots.reshape(N_FSDP, SHARD_TOKENS, TOPK)
    resid_blocks = residual.reshape(N_FSDP, SHARD_TOKENS, MODEL_DIM)
    start_blocks = doc_start.reshape(N_FSDP, SHARD_TOKENS)
    query_key_value = projection_weight.reshape(MODEL_DIM, KEY_HEADS * GROUP_COLUMNS)
    output_weights = output_weight.reshape(KEY_HEADS * QUERY_PER_KV * HEAD_SIZE, MODEL_DIM)

    def one_block(tail_rows, inputs):
        rows_in, ids_in, weights_in, slots_in, resid_in, starts_in, block_index = inputs
        source = (jnp.arange(SHARD_TOKENS, dtype=jnp.int32) // TOK_DEV)[:, None]
        flat_index = ((ids_in * N_EXPERT + source) * CAP + slots_in).astype(jnp.int32)
        slot_table = rows_in.reshape(-1, MODEL_DIM)
        picked = jnp.take(slot_table, flat_index.reshape(-1), axis=0).reshape(SHARD_TOKENS, TOPK, MODEL_DIM)
        combined = lax.optimization_barrier(jnp.sum(weights_in[:, :, None] * picked.astype(jnp.float32), axis=1))
        hidden = (resid_in.astype(jnp.float32) + combined).astype(jnp.bfloat16)
        widened = hidden.astype(jnp.float32)
        normalized_rows = (widened * lax.rsqrt(lax.optimization_barrier(jnp.mean(widened * widened, axis=-1, keepdims=True)) + EPSILON) * norm_gain).astype(jnp.bfloat16)
        projected_rows = jnp.dot(normalized_rows, query_key_value, preferred_element_type=jnp.float32).reshape(SHARD_TOKENS, KEY_HEADS, GROUP_COLUMNS) + projection_bias
        positions = block_index * SHARD_TOKENS + jnp.arange(SHARD_TOKENS, dtype=jnp.int32)
        document_position = positions - starts_in
        query_rows = apply_rotation(projected_rows[..., :QUERY_PER_KV * HEAD_SIZE].reshape(SHARD_TOKENS, KEY_HEADS, QUERY_PER_KV, HEAD_SIZE), document_position).astype(jnp.bfloat16)
        key_rows = apply_rotation(projected_rows[..., QUERY_PER_KV * HEAD_SIZE:(QUERY_PER_KV + 1) * HEAD_SIZE], document_position)
        keys_values = jnp.concatenate([key_rows, projected_rows[..., (QUERY_PER_KV + 1) * HEAD_SIZE:]], axis=-1).astype(jnp.bfloat16)
        extended = jnp.concatenate([tail_rows, keys_values], axis=0)
        key_pos = block_index * SHARD_TOKENS - KEYS_VISIBLE + jnp.arange(KEYS_VISIBLE + SHARD_TOKENS, dtype=jnp.int32)
        attention_result = attend(query_rows, extended, positions, key_pos, starts_in, sinks)
        projection_step = jnp.dot(attention_result.reshape(SHARD_TOKENS, KEY_HEADS * QUERY_PER_KV * HEAD_SIZE), output_weights, preferred_element_type=jnp.float32)
        block_result = (widened + projection_step + b_out).astype(jnp.bfloat16)
        return (keys_values[SHARD_TOKENS - KEYS_VISIBLE:], block_result)
    trailing_start = jnp.zeros((KEYS_VISIBLE, KEY_HEADS, 2 * HEAD_SIZE), jnp.bfloat16)
    unused, results = lax.scan(one_block, trailing_start, (expert_rows, ids_blocks, weight_blocks, slot_blocks, resid_blocks, start_blocks, jnp.arange(N_FSDP, dtype=jnp.int32)))
    return results.reshape(TOKENS, MODEL_DIM)
```

```python
import jax
import jax.numpy as jnp
from jax import lax
from jax.sharding import PartitionSpec as P

HEAD_SIZE = 64
QUERY_PER_KV = 8
TOPK = 4
KEYS_VISIBLE = 128


ROPE_BASE = 150000.0
EPSILON = 1e-05


def passed_along(block, axis, distance):
    devices = range(lax.axis_size(axis))
    route = [(i - distance, i) for i in devices if i - distance in devices]
    return lax.ppermute(block, axis, route)


def apply_rotation(values, positions):
    half_width = values.shape[-1] // 2
    steps_half = jnp.arange(half_width, dtype=jnp.float32)
    frequency = ROPE_BASE ** (-2.0 * steps_half / values.shape[-1])
    angles = positions.astype(jnp.float32)[:, None] * frequency[None, :]
    shape_out = (angles.shape[0],) + (1,) * (values.ndim - 2) + (half_width,)
    cosine = jnp.cos(angles).reshape(shape_out)
    sine_part = jnp.sin(angles).reshape(shape_out)
    front_half = values[..., :half_width]
    back_half = values[..., half_width:]
    return jnp.concatenate(
        [front_half * cosine - back_half * sine_part, back_half * cosine + front_half * sine_part],
        axis=-1,
    )


def attend_block(query_rows, key_rows, query_pos, key_pos, starts, sinks):
    keys_only = key_rows[..., :HEAD_SIZE]
    values_only = key_rows[..., HEAD_SIZE:]
    scores = jnp.einsum(
        "qjgd,kjd->jgqk", query_rows, keys_only, preferred_element_type=jnp.float32
    ) * HEAD_SIZE ** (-0.5)
    allowed = (
        (key_pos[None, :] <= query_pos[:, None])
        & (key_pos[None, :] > query_pos[:, None] - KEYS_VISIBLE)
        & (key_pos[None, :] >= starts[:, None])
    )
    masked = jnp.where(allowed[None, None], scores, -jnp.inf)
    row_peak = jnp.maximum(jnp.max(masked, axis=-1), sinks[:, :, None])
    exponent = jnp.exp(masked - row_peak[..., None])
    denominator = jnp.sum(exponent, axis=-1) + jnp.exp(sinks[:, :, None] - row_peak)
    weights_soft = (exponent / denominator[..., None]).astype(jnp.bfloat16)
    return jnp.einsum(
        "jgqk,kjd->qjgd", weights_soft, values_only, preferred_element_type=jnp.float32
    ).astype(jnp.bfloat16)


def shards(
    expert_rows,
    residual,
    route_ids,
    route_weights,
    route_slots,
    doc_start,
    norm_gain,
    projection_weight,
    projection_bias,
    sinks,
    output_weight,
    b_out,
):
    own_rows = residual.shape[0]
    model_width = residual.shape[1]
    returned = lax.all_to_all(expert_rows, "expert", split_axis=2, concat_axis=1, tiled=True)
    all_experts = returned.shape[1]
    capacity = returned.shape[3]
    hit_expert = route_ids[..., None] == jnp.arange(all_experts, dtype=jnp.int32)
    hit_slot = route_slots[..., None] == jnp.arange(capacity, dtype=jnp.int32)
    hits = hit_expert[..., :, None] & hit_slot[..., None, :]
    select = jnp.sum(jnp.where(hits, route_weights[..., None, None], 0.0), axis=1)
    high = select.astype(jnp.bfloat16)
    low = (select - high.astype(jnp.float32)).astype(jnp.bfloat16)
    both = jnp.concatenate([high, low], axis=0)
    picked = jnp.einsum(
        "txs,xsm->tm", both, returned[0, :, 0], preferred_element_type=jnp.float32
    )
    combined = picked[:own_rows] + picked[own_rows:]
    hidden = (residual.astype(jnp.float32) + combined).astype(jnp.bfloat16)
    widened = hidden.astype(jnp.float32)
    normalized_rows = (
        widened
        * lax.rsqrt(jnp.mean(widened * widened, axis=-1, keepdims=True) + EPSILON)
        * norm_gain
    ).astype(jnp.bfloat16)
    gathered = lax.all_gather(normalized_rows, "expert", axis=0, tiled=True)
    block_rows = gathered.shape[0]
    local_heads = projection_weight.shape[1]
    qkv_full, out_full = (
        lax.all_gather(projection_weight, "fsdp", axis=0, tiled=True),
        lax.all_gather(output_weight, "fsdp", axis=1, tiled=True),
    )
    projected_rows = jnp.dot(
        gathered, qkv_full.reshape(model_width, -1), preferred_element_type=jnp.float32
    )
    projected_rows = projected_rows.reshape(block_rows, local_heads, -1) + projection_bias
    block_start = lax.axis_index("fsdp") * block_rows
    positions = block_start + jnp.arange(block_rows, dtype=jnp.int32)
    document_position = positions - doc_start
    query_rows = apply_rotation(
        projected_rows[..., : QUERY_PER_KV * HEAD_SIZE].reshape(
            block_rows, local_heads, QUERY_PER_KV, HEAD_SIZE
        ),
        document_position,
    ).astype(jnp.bfloat16)
    key_part = apply_rotation(
        projected_rows[..., QUERY_PER_KV * HEAD_SIZE : (QUERY_PER_KV + 1) * HEAD_SIZE],
        document_position,
    )
    keys_values = jnp.concatenate(
        [key_part, projected_rows[..., (QUERY_PER_KV + 1) * HEAD_SIZE :]], axis=-1
    ).astype(jnp.bfloat16)
    before = passed_along(keys_values[block_rows - KEYS_VISIBLE :], "fsdp", 1)
    extended = jnp.concatenate([before, keys_values], axis=0)
    query_block = min(512, block_rows)
    outputs_list = []
    for first_row in range(0, block_rows, query_block):
        key_rows = extended[first_row : first_row + query_block + KEYS_VISIBLE]
        key_pos = (
            block_start
            - KEYS_VISIBLE
            + first_row
            + jnp.arange(query_block + KEYS_VISIBLE, dtype=jnp.int32)
        )
        outputs_list.append(
            attend_block(
                query_rows[first_row : first_row + query_block],
                key_rows,
                positions[first_row : first_row + query_block],
                key_pos,
                doc_start[first_row : first_row + query_block],
                sinks,
            )
        )
    attention_result = jnp.concatenate(outputs_list, axis=0).reshape(block_rows, -1)
    output_weights = out_full.reshape(-1, model_width)
    projection_step = lax.psum_scatter(
        jnp.dot(attention_result, output_weights, preferred_element_type=jnp.float32).astype(
            jnp.bfloat16
        ),
        "expert",
        scatter_dimension=0,
        tiled=True,
    ).astype(jnp.float32)
    return (widened + projection_step + b_out).astype(jnp.bfloat16)


def solution(mesh):
    in_specs = (
        P("fsdp", "expert", None, None, None),
        P(("fsdp", "expert"), None),
        P(("fsdp", "expert"), None),
        P(("fsdp", "expert"), None),
        P(("fsdp", "expert"), None),
        P("fsdp"),
        P(),
        P("fsdp", "expert", None),
        P("expert", None),
        P("expert", None),
        P("expert", "fsdp", None),
        P(),
    )
    out_specs = P(("fsdp", "expert"), None)
    return jax.shard_map(shards, mesh=mesh, in_specs=in_specs, out_specs=out_specs, check_vma=False)
```

```python
import jax
import jax.numpy as jnp
from jax import lax
from jax.sharding import PartitionSpec as P

HEAD_SIZE = 64
QUERY_PER_KV = 8
TOPK = 4
KEYS_VISIBLE = 128


ROPE_BASE = 150000.0
EPSILON = 1e-05


def passed_along(block, axis, distance):
    devices = range(lax.axis_size(axis))
    route = [(i - distance, i) for i in devices if i - distance in devices]
    return lax.ppermute(block, axis, route)


def apply_rotation(values, positions):
    half_width = values.shape[-1] // 2
    steps_half = jnp.arange(half_width, dtype=jnp.float32)
    frequency = ROPE_BASE ** (-2.0 * steps_half / values.shape[-1])
    angles = positions.astype(jnp.float32)[:, None] * frequency[None, :]
    shape_out = (angles.shape[0],) + (1,) * (values.ndim - 2) + (half_width,)
    cosine = jnp.cos(angles).reshape(shape_out)
    sine_part = jnp.sin(angles).reshape(shape_out)
    front_half = values[..., :half_width]
    back_half = values[..., half_width:]
    return jnp.concatenate(
        [front_half * cosine - back_half * sine_part, back_half * cosine + front_half * sine_part],
        axis=-1,
    )


def attend_block(query_rows, key_rows, query_pos, key_pos, starts, sinks):
    keys_only = key_rows[..., :HEAD_SIZE]
    values_only = key_rows[..., HEAD_SIZE:]
    scores = jnp.einsum(
        "qjgd,kjd->jgqk", query_rows, keys_only, preferred_element_type=jnp.float32
    ) * HEAD_SIZE ** (-0.5)
    allowed = (
        (key_pos[None, :] <= query_pos[:, None])
        & (key_pos[None, :] > query_pos[:, None] - KEYS_VISIBLE)
        & (key_pos[None, :] >= starts[:, None])
    )
    masked = jnp.where(allowed[None, None], scores, -jnp.inf)
    row_peak = jnp.maximum(jnp.max(masked, axis=-1), sinks[:, :, None])
    exponent = jnp.exp(masked - row_peak[..., None])
    denominator = jnp.sum(exponent, axis=-1) + jnp.exp(sinks[:, :, None] - row_peak)
    weights_soft = (exponent / denominator[..., None]).astype(jnp.bfloat16)
    return jnp.einsum(
        "jgqk,kjd->qjgd", weights_soft, values_only, preferred_element_type=jnp.float32
    ).astype(jnp.bfloat16)


def gather_fsdp(block):
    count = lax.axis_size("fsdp")
    spread = jnp.broadcast_to(block[None], (count,) + block.shape)
    return lax.all_to_all(spread, "fsdp", split_axis=0, concat_axis=0, tiled=True)


def shards(
    expert_rows,
    residual,
    route_ids,
    route_weights,
    route_slots,
    doc_start,
    norm_gain,
    projection_weight,
    projection_bias,
    sinks,
    output_weight,
    b_out,
):
    own_rows = residual.shape[0]
    model_width = residual.shape[1]
    returned = lax.all_to_all(expert_rows, "expert", split_axis=2, concat_axis=1, tiled=True)
    qkv_full = lax.all_gather(projection_weight, "fsdp", axis=0, tiled=True)
    qkv_full, returned = lax.optimization_barrier((qkv_full, returned))
    all_experts = returned.shape[1]
    capacity = returned.shape[3]
    hit_expert = route_ids[..., None] == jnp.arange(all_experts, dtype=jnp.int32)
    hit_slot = route_slots[..., None] == jnp.arange(capacity, dtype=jnp.int32)
    hits = hit_expert[..., :, None] & hit_slot[..., None, :]
    select = jnp.sum(jnp.where(hits, route_weights[..., None, None], 0.0), axis=1)
    high = select.astype(jnp.bfloat16)
    low = (select - high.astype(jnp.float32)).astype(jnp.bfloat16)
    both = jnp.concatenate([high, low], axis=0)
    picked = jnp.einsum(
        "txs,xsm->tm", both, returned[0, :, 0], preferred_element_type=jnp.float32
    )
    combined = picked[:own_rows] + picked[own_rows:]
    hidden = (residual.astype(jnp.float32) + combined).astype(jnp.bfloat16)
    widened = hidden.astype(jnp.float32)
    normalized_rows = (
        widened
        * lax.rsqrt(jnp.mean(widened * widened, axis=-1, keepdims=True) + EPSILON)
        * norm_gain
    ).astype(jnp.bfloat16)
    gathered = lax.all_gather(normalized_rows, "expert", axis=0, tiled=True)
    out_full = gather_fsdp(output_weight[0])
    out_full, gathered = lax.optimization_barrier((out_full, gathered))
    block_rows = gathered.shape[0]
    local_heads = projection_weight.shape[1]
    projected_rows = jnp.dot(
        gathered, qkv_full.reshape(model_width, -1), preferred_element_type=jnp.float32
    )
    projected_rows = projected_rows.reshape(block_rows, local_heads, -1) + projection_bias
    block_start = lax.axis_index("fsdp") * block_rows
    positions = block_start + jnp.arange(block_rows, dtype=jnp.int32)
    document_position = positions - doc_start
    query_rows = apply_rotation(
        projected_rows[..., : QUERY_PER_KV * HEAD_SIZE].reshape(
            block_rows, local_heads, QUERY_PER_KV, HEAD_SIZE
        ),
        document_position,
    ).astype(jnp.bfloat16)
    key_part = apply_rotation(
        projected_rows[..., QUERY_PER_KV * HEAD_SIZE : (QUERY_PER_KV + 1) * HEAD_SIZE],
        document_position,
    )
    keys_values = jnp.concatenate(
        [key_part, projected_rows[..., (QUERY_PER_KV + 1) * HEAD_SIZE :]], axis=-1
    ).astype(jnp.bfloat16)
    before = passed_along(keys_values[block_rows - KEYS_VISIBLE :], "fsdp", 1)
    extended = jnp.concatenate([before, keys_values], axis=0)
    query_block = min(512, block_rows)
    outputs_list = []
    for first_row in range(0, block_rows, query_block):
        key_rows = extended[first_row : first_row + query_block + KEYS_VISIBLE]
        key_pos = (
            block_start
            - KEYS_VISIBLE
            + first_row
            + jnp.arange(query_block + KEYS_VISIBLE, dtype=jnp.int32)
        )
        outputs_list.append(
            attend_block(
                query_rows[first_row : first_row + query_block],
                key_rows,
                positions[first_row : first_row + query_block],
                key_pos,
                doc_start[first_row : first_row + query_block],
                sinks,
            )
        )
    attention_result = jnp.concatenate(outputs_list, axis=0).reshape(block_rows, -1)
    output_weights = out_full.reshape(-1, model_width)
    projection_step = lax.psum_scatter(
        jnp.dot(attention_result, output_weights, preferred_element_type=jnp.float32).astype(
            jnp.bfloat16
        ),
        "expert",
        scatter_dimension=0,
        tiled=True,
    ).astype(jnp.float32)
    return (widened + projection_step + b_out).astype(jnp.bfloat16)


def solution(mesh):
    in_specs = (
        P("fsdp", "expert", None, None, None),
        P(("fsdp", "expert"), None),
        P(("fsdp", "expert"), None),
        P(("fsdp", "expert"), None),
        P(("fsdp", "expert"), None),
        P("fsdp"),
        P(),
        P("fsdp", "expert", None),
        P("expert", None),
        P("expert", None),
        P("expert", "fsdp", None),
        P(),
    )
    out_specs = P(("fsdp", "expert"), None)
    return jax.shard_map(shards, mesh=mesh, in_specs=in_specs, out_specs=out_specs, check_vma=False)
```

```python
import jax
import jax.numpy as jnp
from jax import lax
from jax.sharding import PartitionSpec as P

HEAD_SIZE = 64
QUERY_PER_KV = 8
TOPK = 4
KEYS_VISIBLE = 128


ROPE_BASE = 150000.0
EPSILON = 1e-05


def passed_along(block, axis, distance):
    devices = range(lax.axis_size(axis))
    route = [(i - distance, i) for i in devices if i - distance in devices]
    return lax.ppermute(block, axis, route)


def apply_rotation(values, positions):
    half_width = values.shape[-1] // 2
    steps_half = jnp.arange(half_width, dtype=jnp.float32)
    frequency = ROPE_BASE ** (-2.0 * steps_half / values.shape[-1])
    angles = positions.astype(jnp.float32)[:, None] * frequency[None, :]
    shape_out = (angles.shape[0],) + (1,) * (values.ndim - 2) + (half_width,)
    cosine = jnp.cos(angles).reshape(shape_out)
    sine_part = jnp.sin(angles).reshape(shape_out)
    front_half = values[..., :half_width]
    back_half = values[..., half_width:]
    return jnp.concatenate(
        [front_half * cosine - back_half * sine_part, back_half * cosine + front_half * sine_part],
        axis=-1,
    )


def attend_block(query_rows, key_rows, query_pos, key_pos, starts, sinks):
    keys_only = key_rows[..., :HEAD_SIZE]
    values_only = key_rows[..., HEAD_SIZE:]
    scores = jnp.einsum(
        "qjgd,kjd->jgqk", query_rows, keys_only, preferred_element_type=jnp.float32
    ) * HEAD_SIZE ** (-0.5)
    allowed = (
        (key_pos[None, :] <= query_pos[:, None])
        & (key_pos[None, :] > query_pos[:, None] - KEYS_VISIBLE)
        & (key_pos[None, :] >= starts[:, None])
    )
    masked = jnp.where(allowed[None, None], scores, -jnp.inf)
    row_peak = jnp.maximum(jnp.max(masked, axis=-1), sinks[:, :, None])
    exponent = jnp.exp(masked - row_peak[..., None])
    denominator = jnp.sum(exponent, axis=-1) + jnp.exp(sinks[:, :, None] - row_peak)
    weights_soft = (exponent / denominator[..., None]).astype(jnp.bfloat16)
    return jnp.einsum(
        "jgqk,kjd->qjgd", weights_soft, values_only, preferred_element_type=jnp.float32
    ).astype(jnp.bfloat16)


def gather_fsdp(block):
    count = lax.axis_size("fsdp")
    spread = jnp.broadcast_to(block[None], (count,) + block.shape)
    return lax.all_to_all(spread, "fsdp", split_axis=0, concat_axis=0, tiled=True)


def shards(
    expert_rows,
    residual,
    route_ids,
    route_weights,
    route_slots,
    doc_start,
    norm_gain,
    projection_weight,
    projection_bias,
    sinks,
    output_weight,
    b_out,
):
    own_rows = residual.shape[0]
    model_width = residual.shape[1]
    returned = lax.all_to_all(expert_rows, "expert", split_axis=2, concat_axis=1, tiled=True)
    qkv_full = lax.all_gather(projection_weight, "fsdp", axis=0, tiled=True)
    qkv_full, returned = lax.optimization_barrier((qkv_full, returned))
    all_experts = returned.shape[1]
    capacity = returned.shape[3]
    hit_expert = route_ids[..., None] == jnp.arange(all_experts, dtype=jnp.int32)
    hit_slot = route_slots[..., None] == jnp.arange(capacity, dtype=jnp.int32)
    hits = hit_expert[..., :, None] & hit_slot[..., None, :]
    select = jnp.sum(jnp.where(hits, route_weights[..., None, None], 0.0), axis=1)
    high = select.astype(jnp.bfloat16)
    low = (select - high.astype(jnp.float32)).astype(jnp.bfloat16)
    both = jnp.concatenate([high, low], axis=0)
    picked = jnp.einsum(
        "txs,xsm->tm", both, returned[0, :, 0], preferred_element_type=jnp.float32
    )
    combined = picked[:own_rows] + picked[own_rows:]
    hidden = (residual.astype(jnp.float32) + combined).astype(jnp.bfloat16)
    widened = hidden.astype(jnp.float32)
    normalized_rows = (
        widened
        * lax.rsqrt(jnp.mean(widened * widened, axis=-1, keepdims=True) + EPSILON)
        * norm_gain
    ).astype(jnp.bfloat16)
    gathered = lax.all_gather(normalized_rows, "expert", axis=0, tiled=True)
    out_full = gather_fsdp(output_weight[0])
    block_rows = gathered.shape[0]
    local_heads = projection_weight.shape[1]
    projected_rows = jnp.dot(
        gathered, qkv_full.reshape(model_width, -1), preferred_element_type=jnp.float32
    )
    projected_rows = projected_rows.reshape(block_rows, local_heads, -1) + projection_bias
    block_start = lax.axis_index("fsdp") * block_rows
    positions = block_start + jnp.arange(block_rows, dtype=jnp.int32)
    document_position = positions - doc_start
    query_rows = apply_rotation(
        projected_rows[..., : QUERY_PER_KV * HEAD_SIZE].reshape(
            block_rows, local_heads, QUERY_PER_KV, HEAD_SIZE
        ),
        document_position,
    ).astype(jnp.bfloat16)
    key_part = apply_rotation(
        projected_rows[..., QUERY_PER_KV * HEAD_SIZE : (QUERY_PER_KV + 1) * HEAD_SIZE],
        document_position,
    )
    keys_values = jnp.concatenate(
        [key_part, projected_rows[..., (QUERY_PER_KV + 1) * HEAD_SIZE :]], axis=-1
    ).astype(jnp.bfloat16)
    before = passed_along(keys_values[block_rows - KEYS_VISIBLE :], "fsdp", 1)
    extended = jnp.concatenate([before, keys_values], axis=0)
    query_block = min(512, block_rows)
    outputs_list = []
    for first_row in range(0, block_rows, query_block):
        key_rows = extended[first_row : first_row + query_block + KEYS_VISIBLE]
        key_pos = (
            block_start
            - KEYS_VISIBLE
            + first_row
            + jnp.arange(query_block + KEYS_VISIBLE, dtype=jnp.int32)
        )
        outputs_list.append(
            attend_block(
                query_rows[first_row : first_row + query_block],
                key_rows,
                positions[first_row : first_row + query_block],
                key_pos,
                doc_start[first_row : first_row + query_block],
                sinks,
            )
        )
    attention_result = jnp.concatenate(outputs_list, axis=0).reshape(block_rows, -1)
    out_full, attention_result = lax.optimization_barrier((out_full, attention_result))
    output_weights = out_full.reshape(-1, model_width)
    projection_step = lax.psum_scatter(
        jnp.dot(attention_result, output_weights, preferred_element_type=jnp.float32).astype(
            jnp.bfloat16
        ),
        "expert",
        scatter_dimension=0,
        tiled=True,
    ).astype(jnp.float32)
    return (widened + projection_step + b_out).astype(jnp.bfloat16)


def solution(mesh):
    in_specs = (
        P("fsdp", "expert", None, None, None),
        P(("fsdp", "expert"), None),
        P(("fsdp", "expert"), None),
        P(("fsdp", "expert"), None),
        P(("fsdp", "expert"), None),
        P("fsdp"),
        P(),
        P("fsdp", "expert", None),
        P("expert", None),
        P("expert", None),
        P("expert", "fsdp", None),
        P(),
    )
    out_specs = P(("fsdp", "expert"), None)
    return jax.shard_map(shards, mesh=mesh, in_specs=in_specs, out_specs=out_specs, check_vma=False)
```

```python
import jax
import jax.numpy as jnp
from jax import lax
from jax.sharding import PartitionSpec as P

HEAD_SIZE = 64
QUERY_PER_KV = 8
TOPK = 4
KEYS_VISIBLE = 128


ROPE_BASE = 150000.0
EPSILON = 1e-05


def passed_along(block, axis, distance):
    devices = range(lax.axis_size(axis))
    route = [(i - distance, i) for i in devices if i - distance in devices]
    return lax.ppermute(block, axis, route)


def apply_rotation(values, positions):
    half_width = values.shape[-1] // 2
    steps_half = jnp.arange(half_width, dtype=jnp.float32)
    frequency = ROPE_BASE ** (-2.0 * steps_half / values.shape[-1])
    angles = positions.astype(jnp.float32)[:, None] * frequency[None, :]
    shape_out = (angles.shape[0],) + (1,) * (values.ndim - 2) + (half_width,)
    cosine = jnp.cos(angles).reshape(shape_out)
    sine_part = jnp.sin(angles).reshape(shape_out)
    front_half = values[..., :half_width]
    back_half = values[..., half_width:]
    return jnp.concatenate(
        [front_half * cosine - back_half * sine_part, back_half * cosine + front_half * sine_part],
        axis=-1,
    )


def attend_block(query_rows, key_rows, query_pos, key_pos, starts, sinks):
    keys_only = key_rows[..., :HEAD_SIZE]
    values_only = key_rows[..., HEAD_SIZE:]
    scores = jnp.einsum(
        "qjgd,kjd->jgqk", query_rows, keys_only, preferred_element_type=jnp.float32
    ) * HEAD_SIZE ** (-0.5)
    allowed = (
        (key_pos[None, :] <= query_pos[:, None])
        & (key_pos[None, :] > query_pos[:, None] - KEYS_VISIBLE)
        & (key_pos[None, :] >= starts[:, None])
    )
    masked = jnp.where(allowed[None, None], scores, -jnp.inf)
    row_peak = jnp.maximum(jnp.max(masked, axis=-1), sinks[:, :, None])
    exponent = jnp.exp(masked - row_peak[..., None])
    denominator = jnp.sum(exponent, axis=-1) + jnp.exp(sinks[:, :, None] - row_peak)
    weights_soft = (exponent / denominator[..., None]).astype(jnp.bfloat16)
    return jnp.einsum(
        "jgqk,kjd->qjgd", weights_soft, values_only, preferred_element_type=jnp.float32
    ).astype(jnp.bfloat16)


def gather_fsdp(block):
    count = lax.axis_size("fsdp")
    spread = jnp.broadcast_to(block[None], (count,) + block.shape)
    return lax.all_to_all(spread, "fsdp", split_axis=0, concat_axis=0, tiled=True)


def shards(
    expert_rows,
    residual,
    route_ids,
    route_weights,
    route_slots,
    doc_start,
    norm_gain,
    projection_weight,
    projection_bias,
    sinks,
    output_weight,
    b_out,
):
    own_rows = residual.shape[0]
    model_width = residual.shape[1]
    qkv_full = lax.all_gather(projection_weight, "fsdp", axis=0, tiled=True)
    local_experts = expert_rows.shape[1]
    half = local_experts // 2
    capacity = expert_rows.shape[3]
    n_exp = lax.axis_size("expert")
    hit_expert = route_ids[..., None] == jnp.arange(n_exp * local_experts, dtype=jnp.int32)
    hit_slot = route_slots[..., None] == jnp.arange(capacity, dtype=jnp.int32)
    hits = hit_expert[..., :, None] & hit_slot[..., None, :]
    select = jnp.sum(jnp.where(hits, route_weights[..., None, None], 0.0), axis=1)
    high = select.astype(jnp.bfloat16)
    low = (select - high.astype(jnp.float32)).astype(jnp.bfloat16)
    both = jnp.concatenate([high, low], axis=0).reshape(
        2 * own_rows, n_exp, local_experts, capacity
    )
    combined = None
    for first in (0, half):
        returned = lax.all_to_all(
            expert_rows[:, first : first + half], "expert", split_axis=2, concat_axis=1, tiled=True
        )
        if first == 0:
            qkv_full, returned = lax.optimization_barrier((qkv_full, returned))
        picked = jnp.einsum(
            "tkxs,kxsm->tm",
            both[:, :, first : first + half],
            returned[0, :, 0].reshape(n_exp, half, capacity, model_width),
            preferred_element_type=jnp.float32,
        )
        picked = picked[:own_rows] + picked[own_rows:]
        combined = picked if combined is None else combined + picked
    hidden = (residual.astype(jnp.float32) + combined).astype(jnp.bfloat16)
    widened = hidden.astype(jnp.float32)
    normalized_rows = (
        widened
        * lax.rsqrt(jnp.mean(widened * widened, axis=-1, keepdims=True) + EPSILON)
        * norm_gain
    ).astype(jnp.bfloat16)
    gathered = lax.all_gather(normalized_rows, "expert", axis=0, tiled=True)
    out_full = gather_fsdp(output_weight[0])
    block_rows = gathered.shape[0]
    local_heads = projection_weight.shape[1]
    projected_rows = jnp.dot(
        gathered, qkv_full.reshape(model_width, -1), preferred_element_type=jnp.float32
    )
    projected_rows = projected_rows.reshape(block_rows, local_heads, -1) + projection_bias
    block_start = lax.axis_index("fsdp") * block_rows
    positions = block_start + jnp.arange(block_rows, dtype=jnp.int32)
    document_position = positions - doc_start
    query_rows = apply_rotation(
        projected_rows[..., : QUERY_PER_KV * HEAD_SIZE].reshape(
            block_rows, local_heads, QUERY_PER_KV, HEAD_SIZE
        ),
        document_position,
    ).astype(jnp.bfloat16)
    key_part = apply_rotation(
        projected_rows[..., QUERY_PER_KV * HEAD_SIZE : (QUERY_PER_KV + 1) * HEAD_SIZE],
        document_position,
    )
    keys_values = jnp.concatenate(
        [key_part, projected_rows[..., (QUERY_PER_KV + 1) * HEAD_SIZE :]], axis=-1
    ).astype(jnp.bfloat16)
    before = passed_along(keys_values[block_rows - KEYS_VISIBLE :], "fsdp", 1)
    extended = jnp.concatenate([before, keys_values], axis=0)
    query_block = min(512, block_rows)
    outputs_list = []
    for first_row in range(0, block_rows, query_block):
        key_rows = extended[first_row : first_row + query_block + KEYS_VISIBLE]
        key_pos = (
            block_start
            - KEYS_VISIBLE
            + first_row
            + jnp.arange(query_block + KEYS_VISIBLE, dtype=jnp.int32)
        )
        outputs_list.append(
            attend_block(
                query_rows[first_row : first_row + query_block],
                key_rows,
                positions[first_row : first_row + query_block],
                key_pos,
                doc_start[first_row : first_row + query_block],
                sinks,
            )
        )
    attention_result = jnp.concatenate(outputs_list, axis=0).reshape(block_rows, -1)
    out_full, attention_result = lax.optimization_barrier((out_full, attention_result))
    output_weights = out_full.reshape(-1, model_width)
    projection_step = lax.psum_scatter(
        jnp.dot(attention_result, output_weights, preferred_element_type=jnp.float32).astype(
            jnp.bfloat16
        ),
        "expert",
        scatter_dimension=0,
        tiled=True,
    ).astype(jnp.float32)
    return (widened + projection_step + b_out).astype(jnp.bfloat16)


def solution(mesh):
    in_specs = (
        P("fsdp", "expert", None, None, None),
        P(("fsdp", "expert"), None),
        P(("fsdp", "expert"), None),
        P(("fsdp", "expert"), None),
        P(("fsdp", "expert"), None),
        P("fsdp"),
        P(),
        P("fsdp", "expert", None),
        P("expert", None),
        P("expert", None),
        P("expert", "fsdp", None),
        P(),
    )
    out_specs = P(("fsdp", "expert"), None)
    return jax.shard_map(shards, mesh=mesh, in_specs=in_specs, out_specs=out_specs, check_vma=False)
```

```python
import jax
import jax.numpy as jnp
from jax import lax
from jax.sharding import PartitionSpec as P

HEAD_SIZE = 64
QUERY_PER_KV = 8
TOPK = 4
KEYS_VISIBLE = 128


ROPE_BASE = 150000.0
EPSILON = 1e-05


def passed_along(block, axis, distance):
    devices = range(lax.axis_size(axis))
    route = [(i - distance, i) for i in devices if i - distance in devices]
    return lax.ppermute(block, axis, route)


def apply_rotation(values, positions):
    half_width = values.shape[-1] // 2
    steps_half = jnp.arange(half_width, dtype=jnp.float32)
    frequency = ROPE_BASE ** (-2.0 * steps_half / values.shape[-1])
    angles = positions.astype(jnp.float32)[:, None] * frequency[None, :]
    shape_out = (angles.shape[0],) + (1,) * (values.ndim - 2) + (half_width,)
    cosine = jnp.cos(angles).reshape(shape_out)
    sine_part = jnp.sin(angles).reshape(shape_out)
    front_half = values[..., :half_width]
    back_half = values[..., half_width:]
    return jnp.concatenate(
        [front_half * cosine - back_half * sine_part, back_half * cosine + front_half * sine_part],
        axis=-1,
    )


def attend_block(query_rows, key_rows, query_pos, key_pos, starts, sinks):
    keys_only = key_rows[..., :HEAD_SIZE]
    values_only = key_rows[..., HEAD_SIZE:]
    scores = jnp.einsum(
        "qjgd,kjd->jgqk", query_rows, keys_only, preferred_element_type=jnp.float32
    ) * HEAD_SIZE ** (-0.5)
    allowed = (
        (key_pos[None, :] <= query_pos[:, None])
        & (key_pos[None, :] > query_pos[:, None] - KEYS_VISIBLE)
        & (key_pos[None, :] >= starts[:, None])
    )
    masked = jnp.where(allowed[None, None], scores, -jnp.inf)
    row_peak = jnp.maximum(jnp.max(masked, axis=-1), sinks[:, :, None])
    exponent = jnp.exp(masked - row_peak[..., None])
    denominator = jnp.sum(exponent, axis=-1) + jnp.exp(sinks[:, :, None] - row_peak)
    weights_soft = (exponent / denominator[..., None]).astype(jnp.bfloat16)
    return jnp.einsum(
        "jgqk,kjd->qjgd", weights_soft, values_only, preferred_element_type=jnp.float32
    ).astype(jnp.bfloat16)


def gather_fsdp(block):
    count = lax.axis_size("fsdp")
    spread = jnp.broadcast_to(block[None], (count,) + block.shape)
    return lax.all_to_all(spread, "fsdp", split_axis=0, concat_axis=0, tiled=True)


def shards(
    expert_rows,
    residual,
    route_ids,
    route_weights,
    route_slots,
    doc_start,
    norm_gain,
    projection_weight,
    projection_bias,
    sinks,
    output_weight,
    b_out,
):
    own_rows = residual.shape[0]
    model_width = residual.shape[1]
    returned = lax.all_to_all(expert_rows, "expert", split_axis=2, concat_axis=1, tiled=True)
    qkv_full = lax.all_gather(projection_weight, "fsdp", axis=0, tiled=True)
    qkv_full, returned = lax.optimization_barrier((qkv_full, returned))
    all_experts = returned.shape[1]
    capacity = returned.shape[3]
    hit_expert = route_ids[..., None] == jnp.arange(all_experts, dtype=jnp.int32)
    hit_slot = route_slots[..., None] == jnp.arange(capacity, dtype=jnp.int32)
    hits = hit_expert[..., :, None] & hit_slot[..., None, :]
    select = jnp.sum(jnp.where(hits, route_weights[..., None, None], 0.0), axis=1)
    high = select.astype(jnp.bfloat16)
    low = (select - high.astype(jnp.float32)).astype(jnp.bfloat16)
    both = jnp.concatenate([high, low], axis=0)
    picked = jnp.einsum(
        "txs,xsm->tm", both, returned[0, :, 0], preferred_element_type=jnp.float32
    )
    combined = picked[:own_rows] + picked[own_rows:]
    hidden = (residual.astype(jnp.float32) + combined).astype(jnp.bfloat16)
    widened = hidden.astype(jnp.float32)
    normalized_rows = (
        widened
        * lax.rsqrt(jnp.mean(widened * widened, axis=-1, keepdims=True) + EPSILON)
        * norm_gain
    ).astype(jnp.bfloat16)
    gathered = lax.all_gather(normalized_rows, "expert", axis=0, tiled=True)
    out_full = gather_fsdp(output_weight[0])
    block_rows = gathered.shape[0]
    local_heads = projection_weight.shape[1]
    projected_rows = jnp.dot(
        gathered, qkv_full.reshape(model_width, -1), preferred_element_type=jnp.float32
    )
    projected_rows = projected_rows.reshape(block_rows, local_heads, -1) + projection_bias
    block_start = lax.axis_index("fsdp") * block_rows
    positions = block_start + jnp.arange(block_rows, dtype=jnp.int32)
    document_position = positions - doc_start
    query_rows = apply_rotation(
        projected_rows[..., : QUERY_PER_KV * HEAD_SIZE].reshape(
            block_rows, local_heads, QUERY_PER_KV, HEAD_SIZE
        ),
        document_position,
    ).astype(jnp.bfloat16)
    key_part = apply_rotation(
        projected_rows[..., QUERY_PER_KV * HEAD_SIZE : (QUERY_PER_KV + 1) * HEAD_SIZE],
        document_position,
    )
    keys_values = jnp.concatenate(
        [key_part, projected_rows[..., (QUERY_PER_KV + 1) * HEAD_SIZE :]], axis=-1
    ).astype(jnp.bfloat16)
    before = passed_along(keys_values[block_rows - KEYS_VISIBLE :], "fsdp", 1)
    query_block = min(512, block_rows)

    def one_query_block(first_row, key_rows):
        key_pos = (
            block_start
            - KEYS_VISIBLE
            + first_row
            + jnp.arange(query_block + KEYS_VISIBLE, dtype=jnp.int32)
        )
        return attend_block(
            query_rows[first_row : first_row + query_block],
            key_rows,
            positions[first_row : first_row + query_block],
            key_pos,
            doc_start[first_row : first_row + query_block],
            sinks,
        )

    later = [
        one_query_block(first_row, keys_values[first_row - KEYS_VISIBLE : first_row + query_block])
        for first_row in range(query_block, block_rows, query_block)
    ]
    before, later = lax.optimization_barrier((before, later))
    extended = jnp.concatenate([before, keys_values[: query_block]], axis=0)
    outputs_list = [one_query_block(0, extended)] + later
    attention_result = jnp.concatenate(outputs_list, axis=0).reshape(block_rows, -1)
    out_full, attention_result = lax.optimization_barrier((out_full, attention_result))
    output_weights = out_full.reshape(-1, model_width)
    projection_step = lax.psum_scatter(
        jnp.dot(attention_result, output_weights, preferred_element_type=jnp.float32).astype(
            jnp.bfloat16
        ),
        "expert",
        scatter_dimension=0,
        tiled=True,
    ).astype(jnp.float32)
    return (widened + projection_step + b_out).astype(jnp.bfloat16)


def solution(mesh):
    in_specs = (
        P("fsdp", "expert", None, None, None),
        P(("fsdp", "expert"), None),
        P(("fsdp", "expert"), None),
        P(("fsdp", "expert"), None),
        P(("fsdp", "expert"), None),
        P("fsdp"),
        P(),
        P("fsdp", "expert", None),
        P("expert", None),
        P("expert", None),
        P("expert", "fsdp", None),
        P(),
    )
    out_specs = P(("fsdp", "expert"), None)
    return jax.shard_map(shards, mesh=mesh, in_specs=in_specs, out_specs=out_specs, check_vma=False)
```

```python
import jax
import jax.numpy as jnp
from jax import lax
from jax.experimental.layout import Layout, with_layout_constraint
from jax.sharding import PartitionSpec as P

HEAD_SIZE = 64
QUERY_PER_KV = 8
TOPK = 4
KEYS_VISIBLE = 128


ROPE_BASE = 150000.0
EPSILON = 1e-05


def passed_along(block, axis, distance):
    devices = range(lax.axis_size(axis))
    route = [(i - distance, i) for i in devices if i - distance in devices]
    return lax.ppermute(block, axis, route)


def apply_rotation(values, positions):
    half_width = values.shape[-1] // 2
    steps_half = jnp.arange(half_width, dtype=jnp.float32)
    frequency = ROPE_BASE ** (-2.0 * steps_half / values.shape[-1])
    angles = positions.astype(jnp.float32)[:, None] * frequency[None, :]
    shape_out = (angles.shape[0],) + (1,) * (values.ndim - 2) + (half_width,)
    cosine = jnp.cos(angles).reshape(shape_out)
    sine_part = jnp.sin(angles).reshape(shape_out)
    front_half = values[..., :half_width]
    back_half = values[..., half_width:]
    return jnp.concatenate(
        [front_half * cosine - back_half * sine_part, back_half * cosine + front_half * sine_part],
        axis=-1,
    )


def attend_block(query_rows, key_rows, query_pos, key_pos, starts, sinks):
    keys_only = key_rows[..., :HEAD_SIZE]
    values_only = key_rows[..., HEAD_SIZE:]
    scores = jnp.einsum(
        "qjgd,kjd->jgqk", query_rows, keys_only, preferred_element_type=jnp.float32
    ) * HEAD_SIZE ** (-0.5)
    allowed = (
        (key_pos[None, :] <= query_pos[:, None])
        & (key_pos[None, :] > query_pos[:, None] - KEYS_VISIBLE)
        & (key_pos[None, :] >= starts[:, None])
    )
    masked = jnp.where(allowed[None, None], scores, -jnp.inf)
    row_peak = jnp.maximum(jnp.max(masked, axis=-1), sinks[:, :, None])
    exponent = jnp.exp(masked - row_peak[..., None])
    denominator = jnp.sum(exponent, axis=-1) + jnp.exp(sinks[:, :, None] - row_peak)
    weights_soft = (exponent / denominator[..., None]).astype(jnp.bfloat16)
    return jnp.einsum(
        "jgqk,kjd->qjgd", weights_soft, values_only, preferred_element_type=jnp.float32
    ).astype(jnp.bfloat16)


def gather_fsdp(block):
    count = lax.axis_size("fsdp")
    spread = jnp.broadcast_to(block[None], (count,) + block.shape)
    return lax.all_to_all(spread, "fsdp", split_axis=0, concat_axis=0, tiled=True)


def shards(
    expert_rows,
    residual,
    route_ids,
    route_weights,
    route_slots,
    doc_start,
    norm_gain,
    projection_weight,
    projection_bias,
    sinks,
    output_weight,
    b_out,
):
    own_rows = residual.shape[0]
    model_width = residual.shape[1]
    returned = lax.all_to_all(expert_rows, "expert", split_axis=2, concat_axis=1, tiled=True)
    qkv_full = lax.all_gather(projection_weight, "fsdp", axis=0, tiled=True)
    qkv_full, returned = lax.optimization_barrier((qkv_full, returned))
    all_experts = returned.shape[1]
    capacity = returned.shape[3]
    hit_expert = route_ids[..., None] == jnp.arange(all_experts, dtype=jnp.int32)
    hit_slot = route_slots[..., None] == jnp.arange(capacity, dtype=jnp.int32)
    hits = hit_expert[..., :, None] & hit_slot[..., None, :]
    select = jnp.sum(jnp.where(hits, route_weights[..., None, None], 0.0), axis=1)
    high = select.astype(jnp.bfloat16)
    low = (select - high.astype(jnp.float32)).astype(jnp.bfloat16)
    both = jnp.concatenate([high, low], axis=0)
    picked = jnp.einsum(
        "txs,xsm->tm", both, returned[0, :, 0], preferred_element_type=jnp.float32
    )
    combined = picked[:own_rows] + picked[own_rows:]
    hidden = (residual.astype(jnp.float32) + combined).astype(jnp.bfloat16)
    widened = hidden.astype(jnp.float32)
    normalized_rows = (
        widened
        * lax.rsqrt(jnp.mean(widened * widened, axis=-1, keepdims=True) + EPSILON)
        * norm_gain
    ).astype(jnp.bfloat16)
    gathered = lax.all_gather(normalized_rows, "expert", axis=0, tiled=True)
    out_full = gather_fsdp(output_weight[0])
    block_rows = gathered.shape[0]
    local_heads = projection_weight.shape[1]
    projected_rows = jnp.dot(
        gathered, qkv_full.reshape(model_width, -1), preferred_element_type=jnp.float32
    )
    projected_rows = projected_rows.reshape(block_rows, local_heads, -1) + projection_bias
    block_start = lax.axis_index("fsdp") * block_rows
    positions = block_start + jnp.arange(block_rows, dtype=jnp.int32)
    document_position = positions - doc_start
    query_rows = apply_rotation(
        projected_rows[..., : QUERY_PER_KV * HEAD_SIZE].reshape(
            block_rows, local_heads, QUERY_PER_KV, HEAD_SIZE
        ),
        document_position,
    ).astype(jnp.bfloat16)
    key_part = apply_rotation(
        projected_rows[..., QUERY_PER_KV * HEAD_SIZE : (QUERY_PER_KV + 1) * HEAD_SIZE],
        document_position,
    )
    keys_values = jnp.concatenate(
        [key_part, projected_rows[..., (QUERY_PER_KV + 1) * HEAD_SIZE :]], axis=-1
    ).astype(jnp.bfloat16)
    before = passed_along(keys_values[block_rows - KEYS_VISIBLE :], "fsdp", 1)
    query_block = min(512, block_rows)

    def one_query_block(first_row, key_rows):
        key_pos = (
            block_start
            - KEYS_VISIBLE
            + first_row
            + jnp.arange(query_block + KEYS_VISIBLE, dtype=jnp.int32)
        )
        return attend_block(
            query_rows[first_row : first_row + query_block],
            key_rows,
            positions[first_row : first_row + query_block],
            key_pos,
            doc_start[first_row : first_row + query_block],
            sinks,
        )

    later = [
        one_query_block(first_row, keys_values[first_row - KEYS_VISIBLE : first_row + query_block])
        for first_row in range(query_block, block_rows, query_block)
    ]
    before, later = lax.optimization_barrier((before, later))
    extended = jnp.concatenate([before, keys_values[: query_block]], axis=0)
    outputs_list = [one_query_block(0, extended)] + later
    attention_result = jnp.concatenate(outputs_list, axis=0).reshape(block_rows, -1)
    out_full, attention_result = lax.optimization_barrier((out_full, attention_result))
    output_weights = out_full.reshape(-1, model_width)
    projection_step = with_layout_constraint(
        jnp.dot(attention_result, output_weights, preferred_element_type=jnp.float32).astype(
            jnp.bfloat16
        ),
        Layout((0, 1)),
    )
    projection_step = lax.psum_scatter(
        projection_step,
        "expert",
        scatter_dimension=0,
        tiled=True,
    ).astype(jnp.float32)
    return (widened + projection_step + b_out).astype(jnp.bfloat16)


def solution(mesh):
    in_specs = (
        P("fsdp", "expert", None, None, None),
        P(("fsdp", "expert"), None),
        P(("fsdp", "expert"), None),
        P(("fsdp", "expert"), None),
        P(("fsdp", "expert"), None),
        P("fsdp"),
        P(),
        P("fsdp", "expert", None),
        P("expert", None),
        P("expert", None),
        P("expert", "fsdp", None),
        P(),
    )
    out_specs = P(("fsdp", "expert"), None)
    return jax.shard_map(shards, mesh=mesh, in_specs=in_specs, out_specs=out_specs, check_vma=False)
```

```python
import jax
import jax.numpy as jnp
from jax import lax
from jax.experimental.layout import Layout, with_layout_constraint
from jax.sharding import PartitionSpec as P

HEAD_SIZE = 64
QUERY_PER_KV = 8
TOPK = 4
KEYS_VISIBLE = 128


ROPE_BASE = 150000.0
EPSILON = 1e-05


def passed_along(block, axis, distance):
    devices = range(lax.axis_size(axis))
    route = [(i - distance, i) for i in devices if i - distance in devices]
    return lax.ppermute(block, axis, route)


def apply_rotation(values, positions):
    half_width = values.shape[-1] // 2
    steps_half = jnp.arange(half_width, dtype=jnp.float32)
    frequency = ROPE_BASE ** (-2.0 * steps_half / values.shape[-1])
    angles = positions.astype(jnp.float32)[:, None] * frequency[None, :]
    shape_out = (angles.shape[0],) + (1,) * (values.ndim - 2) + (half_width,)
    cosine = jnp.cos(angles).reshape(shape_out)
    sine_part = jnp.sin(angles).reshape(shape_out)
    front_half = values[..., :half_width]
    back_half = values[..., half_width:]
    return jnp.concatenate(
        [front_half * cosine - back_half * sine_part, back_half * cosine + front_half * sine_part],
        axis=-1,
    )


def attend_block(query_rows, key_rows, query_pos, key_pos, starts, sinks):
    keys_only = key_rows[..., :HEAD_SIZE]
    values_only = key_rows[..., HEAD_SIZE:]
    scores = jnp.einsum(
        "qjgd,kjd->jgqk", query_rows, keys_only, preferred_element_type=jnp.float32
    ) * HEAD_SIZE ** (-0.5)
    allowed = (
        (key_pos[None, :] <= query_pos[:, None])
        & (key_pos[None, :] > query_pos[:, None] - KEYS_VISIBLE)
        & (key_pos[None, :] >= starts[:, None])
    )
    masked = jnp.where(allowed[None, None], scores, -jnp.inf)
    row_peak = jnp.maximum(jnp.max(masked, axis=-1), sinks[:, :, None])
    exponent = jnp.exp(masked - row_peak[..., None])
    denominator = jnp.sum(exponent, axis=-1) + jnp.exp(sinks[:, :, None] - row_peak)
    weights_soft = (exponent / denominator[..., None]).astype(jnp.bfloat16)
    return jnp.einsum(
        "jgqk,kjd->qjgd", weights_soft, values_only, preferred_element_type=jnp.float32
    ).astype(jnp.bfloat16)


def gather_fsdp(block):
    count = lax.axis_size("fsdp")
    spread = jnp.broadcast_to(block[None], (count,) + block.shape)
    return lax.all_to_all(spread, "fsdp", split_axis=0, concat_axis=0, tiled=True)


def shards(
    expert_rows,
    residual,
    route_ids,
    route_weights,
    route_slots,
    doc_start,
    norm_gain,
    projection_weight,
    projection_bias,
    sinks,
    output_weight,
    b_out,
):
    own_rows = residual.shape[0]
    model_width = residual.shape[1]
    returned = lax.all_to_all(expert_rows, "expert", split_axis=2, concat_axis=1, tiled=True)
    qkv_full = lax.all_gather(projection_weight, "fsdp", axis=0, tiled=True)
    qkv_full, returned = lax.optimization_barrier((qkv_full, returned))
    all_experts = returned.shape[1]
    capacity = returned.shape[3]
    hit_expert = route_ids[..., None] == jnp.arange(all_experts, dtype=jnp.int32)
    hit_slot = route_slots[..., None] == jnp.arange(capacity, dtype=jnp.int32)
    hits = hit_expert[..., :, None] & hit_slot[..., None, :]
    select = jnp.sum(jnp.where(hits, route_weights[..., None, None], 0.0), axis=1)
    high = select.astype(jnp.bfloat16)
    low = (select - high.astype(jnp.float32)).astype(jnp.bfloat16)
    both = jnp.concatenate([high, low], axis=0)
    picked = jnp.einsum(
        "txs,xsm->tm", both, returned[0, :, 0], preferred_element_type=jnp.float32
    )
    combined = picked[:own_rows] + picked[own_rows:]
    hidden = (residual.astype(jnp.float32) + combined).astype(jnp.bfloat16)
    widened = hidden.astype(jnp.float32)
    normalized_rows = (
        widened
        * lax.rsqrt(jnp.mean(widened * widened, axis=-1, keepdims=True) + EPSILON)
        * norm_gain
    ).astype(jnp.bfloat16)
    gathered = lax.all_gather(normalized_rows, "expert", axis=0, tiled=True)
    out_full = gather_fsdp(output_weight[0])
    block_rows = gathered.shape[0]
    local_heads = projection_weight.shape[1]
    projected_rows = jnp.dot(
        gathered, qkv_full.reshape(model_width, -1), preferred_element_type=jnp.float32
    )
    projected_rows = projected_rows.reshape(block_rows, local_heads, -1) + projection_bias
    block_start = lax.axis_index("fsdp") * block_rows
    positions = block_start + jnp.arange(block_rows, dtype=jnp.int32)
    document_position = positions - doc_start
    query_rows = apply_rotation(
        projected_rows[..., : QUERY_PER_KV * HEAD_SIZE].reshape(
            block_rows, local_heads, QUERY_PER_KV, HEAD_SIZE
        ),
        document_position,
    ).astype(jnp.bfloat16)
    key_part = apply_rotation(
        projected_rows[..., QUERY_PER_KV * HEAD_SIZE : (QUERY_PER_KV + 1) * HEAD_SIZE],
        document_position,
    )
    keys_values = jnp.concatenate(
        [key_part, projected_rows[..., (QUERY_PER_KV + 1) * HEAD_SIZE :]], axis=-1
    ).astype(jnp.bfloat16)
    before = passed_along(keys_values[block_rows - KEYS_VISIBLE :], "fsdp", 1)
    head_rows = min(KEYS_VISIBLE, block_rows)
    body_rows = (block_rows - head_rows) // 2

    def one_query_block(first_row, query_count, key_rows):
        key_pos = (
            block_start
            - KEYS_VISIBLE
            + first_row
            + jnp.arange(query_count + KEYS_VISIBLE, dtype=jnp.int32)
        )
        return attend_block(
            query_rows[first_row : first_row + query_count],
            key_rows,
            positions[first_row : first_row + query_count],
            key_pos,
            doc_start[first_row : first_row + query_count],
            sinks,
        )

    later = [
        one_query_block(
            first_row,
            query_count,
            keys_values[first_row - KEYS_VISIBLE : first_row + query_count],
        )
        for first_row, query_count in (
            (head_rows, body_rows),
            (head_rows + body_rows, block_rows - head_rows - body_rows),
        )
    ]
    before, later = lax.optimization_barrier((before, later))
    extended = jnp.concatenate([before, keys_values[:head_rows]], axis=0)
    outputs_list = [one_query_block(0, head_rows, extended)] + later
    attention_result = jnp.concatenate(outputs_list, axis=0).reshape(block_rows, -1)
    out_full, attention_result = lax.optimization_barrier((out_full, attention_result))
    output_weights = out_full.reshape(-1, model_width)
    projection_step = with_layout_constraint(
        jnp.dot(attention_result, output_weights, preferred_element_type=jnp.float32).astype(
            jnp.bfloat16
        ),
        Layout((0, 1)),
    )
    projection_step = lax.psum_scatter(
        projection_step,
        "expert",
        scatter_dimension=0,
        tiled=True,
    ).astype(jnp.float32)
    return (widened + projection_step + b_out).astype(jnp.bfloat16)


def solution(mesh):
    in_specs = (
        P("fsdp", "expert", None, None, None),
        P(("fsdp", "expert"), None),
        P(("fsdp", "expert"), None),
        P(("fsdp", "expert"), None),
        P(("fsdp", "expert"), None),
        P("fsdp"),
        P(),
        P("fsdp", "expert", None),
        P("expert", None),
        P("expert", None),
        P("expert", "fsdp", None),
        P(),
    )
    out_specs = P(("fsdp", "expert"), None)
    return jax.shard_map(shards, mesh=mesh, in_specs=in_specs, out_specs=out_specs, check_vma=False)
```

```python
import jax
import jax.numpy as jnp
from jax import lax
from jax.experimental.layout import Layout, with_layout_constraint
from jax.sharding import PartitionSpec as P

HEAD_SIZE = 64
QUERY_PER_KV = 8
TOPK = 4
KEYS_VISIBLE = 128


ROPE_BASE = 150000.0
EPSILON = 1e-05


def passed_along(block, axis, distance):
    devices = range(lax.axis_size(axis))
    route = [(i - distance, i) for i in devices if i - distance in devices]
    return lax.ppermute(block, axis, route)


def apply_rotation(values, positions):
    half_width = values.shape[-1] // 2
    steps_half = jnp.arange(half_width, dtype=jnp.float32)
    frequency = ROPE_BASE ** (-2.0 * steps_half / values.shape[-1])
    angles = positions.astype(jnp.float32)[:, None] * frequency[None, :]
    shape_out = (angles.shape[0],) + (1,) * (values.ndim - 2) + (half_width,)
    cosine = jnp.cos(angles).reshape(shape_out)
    sine_part = jnp.sin(angles).reshape(shape_out)
    front_half = values[..., :half_width]
    back_half = values[..., half_width:]
    return jnp.concatenate(
        [front_half * cosine - back_half * sine_part, back_half * cosine + front_half * sine_part],
        axis=-1,
    )


def attend_block(query_rows, key_rows, query_pos, key_pos, starts, sinks):
    keys_only = key_rows[..., :HEAD_SIZE]
    values_only = key_rows[..., HEAD_SIZE:]
    scores = jnp.einsum(
        "qjgd,kjd->jgqk", query_rows, keys_only, preferred_element_type=jnp.float32
    ) * HEAD_SIZE ** (-0.5)
    allowed = (
        (key_pos[None, :] <= query_pos[:, None])
        & (key_pos[None, :] > query_pos[:, None] - KEYS_VISIBLE)
        & (key_pos[None, :] >= starts[:, None])
    )
    masked = jnp.where(allowed[None, None], scores, -jnp.inf)
    row_peak = jnp.maximum(jnp.max(masked, axis=-1), sinks[:, :, None])
    exponent = jnp.exp(masked - row_peak[..., None])
    denominator = jnp.sum(exponent, axis=-1) + jnp.exp(sinks[:, :, None] - row_peak)
    weights_soft = (exponent / denominator[..., None]).astype(jnp.bfloat16)
    return jnp.einsum(
        "jgqk,kjd->qjgd", weights_soft, values_only, preferred_element_type=jnp.float32
    ).astype(jnp.bfloat16)


def gather_fsdp(block):
    count = lax.axis_size("fsdp")
    spread = jnp.broadcast_to(block[None], (count,) + block.shape)
    return lax.all_to_all(spread, "fsdp", split_axis=0, concat_axis=0, tiled=True)


def shards(
    expert_rows,
    residual,
    route_ids,
    route_weights,
    route_slots,
    doc_start,
    norm_gain,
    projection_weight,
    projection_bias,
    sinks,
    output_weight,
    b_out,
):
    own_rows = residual.shape[0]
    model_width = residual.shape[1]
    returned = lax.all_to_all(expert_rows, "expert", split_axis=2, concat_axis=1, tiled=True)
    qkv_full = lax.all_gather(projection_weight, "fsdp", axis=0, tiled=True)
    qkv_full, returned = lax.optimization_barrier((qkv_full, returned))
    all_experts = returned.shape[1]
    capacity = returned.shape[3]
    hit_expert = route_ids[..., None] == jnp.arange(all_experts, dtype=jnp.int32)
    hit_slot = route_slots[..., None] == jnp.arange(capacity, dtype=jnp.int32)
    hits = hit_expert[..., :, None] & hit_slot[..., None, :]
    select = jnp.sum(jnp.where(hits, route_weights[..., None, None], 0.0), axis=1)
    high = select.astype(jnp.bfloat16)
    low = (select - high.astype(jnp.float32)).astype(jnp.bfloat16)
    both = jnp.concatenate([high, low], axis=0)
    picked = jnp.einsum(
        "txs,xsm->tm", both, returned[0, :, 0], preferred_element_type=jnp.float32
    )
    combined = picked[:own_rows] + picked[own_rows:]
    hidden = (residual.astype(jnp.float32) + combined).astype(jnp.bfloat16)
    widened = hidden.astype(jnp.float32)
    normalized_rows = (
        widened
        * lax.rsqrt(jnp.mean(widened * widened, axis=-1, keepdims=True) + EPSILON)
        * norm_gain
    ).astype(jnp.bfloat16)
    gathered = lax.all_gather(normalized_rows, "expert", axis=0, tiled=True)
    out_full = gather_fsdp(output_weight[0])
    block_rows = gathered.shape[0]
    local_heads = projection_weight.shape[1]
    projected_rows = jnp.dot(
        gathered, qkv_full.reshape(model_width, -1), preferred_element_type=jnp.float32
    )
    projected_rows = projected_rows.reshape(block_rows, local_heads, -1) + projection_bias
    block_start = lax.axis_index("fsdp") * block_rows
    positions = block_start + jnp.arange(block_rows, dtype=jnp.int32)
    document_position = positions - doc_start
    query_rows = apply_rotation(
        projected_rows[..., : QUERY_PER_KV * HEAD_SIZE].reshape(
            block_rows, local_heads, QUERY_PER_KV, HEAD_SIZE
        ),
        document_position,
    ).astype(jnp.bfloat16)
    key_part = apply_rotation(
        projected_rows[..., QUERY_PER_KV * HEAD_SIZE : (QUERY_PER_KV + 1) * HEAD_SIZE],
        document_position,
    )
    keys_values = jnp.concatenate(
        [key_part, projected_rows[..., (QUERY_PER_KV + 1) * HEAD_SIZE :]], axis=-1
    ).astype(jnp.bfloat16)
    before = passed_along(keys_values[block_rows - KEYS_VISIBLE :], "fsdp", 1)
    head_rows = min(KEYS_VISIBLE, block_rows)
    body_rows = (block_rows - head_rows) // 2

    def one_query_block(first_row, query_count, key_rows):
        key_pos = (
            block_start
            - KEYS_VISIBLE
            + first_row
            + jnp.arange(query_count + KEYS_VISIBLE, dtype=jnp.int32)
        )
        return attend_block(
            query_rows[first_row : first_row + query_count],
            key_rows,
            positions[first_row : first_row + query_count],
            key_pos,
            doc_start[first_row : first_row + query_count],
            sinks,
        )

    later = [
        one_query_block(
            first_row,
            query_count,
            keys_values[first_row - KEYS_VISIBLE : first_row + query_count],
        )
        for first_row, query_count in (
            (head_rows, body_rows),
            (head_rows + body_rows, block_rows - head_rows - body_rows),
        )
    ]
    before, later = lax.optimization_barrier((before, later))
    extended = jnp.concatenate([before, keys_values[:head_rows]], axis=0)
    outputs_list = [one_query_block(0, head_rows, extended)] + later
    attention_result = jnp.concatenate(outputs_list, axis=0).reshape(block_rows, -1)
    out_full, attention_result = lax.optimization_barrier((out_full, attention_result))
    output_weights = out_full.reshape(-1, model_width)
    n_exp = lax.axis_size("expert")
    split_rows = own_rows // 2
    by_owner = attention_result.reshape(n_exp, own_rows, -1)

    def project(rows):
        return with_layout_constraint(
            jnp.dot(
                rows.reshape(-1, rows.shape[-1]), output_weights, preferred_element_type=jnp.float32
            ).astype(jnp.bfloat16),
            Layout((0, 1)),
        )

    front = lax.psum_scatter(
        project(by_owner[:, :split_rows]), "expert", scatter_dimension=0, tiled=True
    )
    back = project(by_owner[:, split_rows:]).reshape(n_exp, own_rows - split_rows, model_width)
    back = lax.all_to_all(back, "expert", split_axis=0, concat_axis=0, tiled=True)
    back = jnp.sum(back.astype(jnp.float32), axis=0)
    projection_step = jnp.concatenate([front.astype(jnp.float32), back], axis=0)
    return (widened + projection_step + b_out).astype(jnp.bfloat16)


def solution(mesh):
    in_specs = (
        P("fsdp", "expert", None, None, None),
        P(("fsdp", "expert"), None),
        P(("fsdp", "expert"), None),
        P(("fsdp", "expert"), None),
        P(("fsdp", "expert"), None),
        P("fsdp"),
        P(),
        P("fsdp", "expert", None),
        P("expert", None),
        P("expert", None),
        P("expert", "fsdp", None),
        P(),
    )
    out_specs = P(("fsdp", "expert"), None)
    return jax.shard_map(shards, mesh=mesh, in_specs=in_specs, out_specs=out_specs, check_vma=False)
```

```python
import jax
import jax.numpy as jnp
from jax import lax
from jax.experimental.layout import Layout, with_layout_constraint
from jax.sharding import Mesh, PartitionSpec as P

HEAD_SIZE = 64
QUERY_PER_KV = 8
TOPK = 4
KEYS_VISIBLE = 128


ROPE_BASE = 150000.0
EPSILON = 1e-05


def passed_along(block, axis, distance):
    devices = range(lax.axis_size(axis))
    route = [(i - distance, i) for i in devices if i - distance in devices]
    return lax.ppermute(block, axis, route)


def apply_rotation(values, positions):
    half_width = values.shape[-1] // 2
    steps_half = jnp.arange(half_width, dtype=jnp.float32)
    frequency = ROPE_BASE ** (-2.0 * steps_half / values.shape[-1])
    angles = positions.astype(jnp.float32)[:, None] * frequency[None, :]
    shape_out = (angles.shape[0],) + (1,) * (values.ndim - 2) + (half_width,)
    cosine = jnp.cos(angles).reshape(shape_out)
    sine_part = jnp.sin(angles).reshape(shape_out)
    front_half = values[..., :half_width]
    back_half = values[..., half_width:]
    return jnp.concatenate(
        [front_half * cosine - back_half * sine_part, back_half * cosine + front_half * sine_part],
        axis=-1,
    )


def attend_block(query_rows, key_rows, query_pos, key_pos, starts, sinks):
    keys_only = key_rows[..., :HEAD_SIZE]
    values_only = key_rows[..., HEAD_SIZE:]
    scores = jnp.einsum(
        "qjgd,kjd->jgqk", query_rows, keys_only, preferred_element_type=jnp.float32
    ) * HEAD_SIZE ** (-0.5)
    allowed = (
        (key_pos[None, :] <= query_pos[:, None])
        & (key_pos[None, :] > query_pos[:, None] - KEYS_VISIBLE)
        & (key_pos[None, :] >= starts[:, None])
    )
    masked = jnp.where(allowed[None, None], scores, -jnp.inf)
    row_peak = jnp.maximum(jnp.max(masked, axis=-1), sinks[:, :, None])
    exponent = jnp.exp(masked - row_peak[..., None])
    denominator = jnp.sum(exponent, axis=-1) + jnp.exp(sinks[:, :, None] - row_peak)
    weights_soft = (exponent / denominator[..., None]).astype(jnp.bfloat16)
    return jnp.einsum(
        "jgqk,kjd->qjgd", weights_soft, values_only, preferred_element_type=jnp.float32
    ).astype(jnp.bfloat16)


def gather_fsdp(block):
    count = lax.axis_size("fsdp")
    spread = jnp.broadcast_to(block[None], (count,) + block.shape)
    return lax.all_to_all(spread, "fsdp", split_axis=0, concat_axis=0, tiled=True)


def shards(
    expert_rows,
    residual,
    route_ids,
    route_weights,
    route_slots,
    doc_start,
    norm_gain,
    projection_weight,
    projection_bias,
    sinks,
    output_weight,
    b_out,
):
    own_rows = residual.shape[0]
    model_width = residual.shape[1]
    returned = lax.all_to_all(expert_rows, ("ey", "ec"), split_axis=2, concat_axis=1, tiled=True)
    qkv_full = lax.all_gather(projection_weight, "fsdp", axis=0, tiled=True)
    qkv_full, returned = lax.optimization_barrier((qkv_full, returned))
    all_experts = returned.shape[1]
    capacity = returned.shape[3]
    hit_expert = route_ids[..., None] == jnp.arange(all_experts, dtype=jnp.int32)
    hit_slot = route_slots[..., None] == jnp.arange(capacity, dtype=jnp.int32)
    hits = hit_expert[..., :, None] & hit_slot[..., None, :]
    select = jnp.sum(jnp.where(hits, route_weights[..., None, None], 0.0), axis=1)
    high = select.astype(jnp.bfloat16)
    low = (select - high.astype(jnp.float32)).astype(jnp.bfloat16)
    both = jnp.concatenate([high, low], axis=0)
    picked = jnp.einsum(
        "txs,xsm->tm", both, returned[0, :, 0], preferred_element_type=jnp.float32
    )
    combined = picked[:own_rows] + picked[own_rows:]
    hidden = (residual.astype(jnp.float32) + combined).astype(jnp.bfloat16)
    widened = hidden.astype(jnp.float32)
    normalized_rows = (
        widened
        * lax.rsqrt(jnp.mean(widened * widened, axis=-1, keepdims=True) + EPSILON)
        * norm_gain
    ).astype(jnp.bfloat16)
    own_parity = lax.all_gather(normalized_rows[None], "ey", axis=0, tiled=True)
    other_parity = lax.ppermute(own_parity, "ec", [(0, 1), (1, 0)])
    first_core = lax.axis_index("ec") == 0
    gathered = jnp.stack(
        [
            jnp.where(first_core, own_parity, other_parity),
            jnp.where(first_core, other_parity, own_parity),
        ],
        axis=1,
    ).reshape(-1, model_width)
    out_full = gather_fsdp(output_weight[0])
    block_rows = gathered.shape[0]
    local_heads = projection_weight.shape[1]
    projected_rows = jnp.dot(
        gathered, qkv_full.reshape(model_width, -1), preferred_element_type=jnp.float32
    )
    projected_rows = projected_rows.reshape(block_rows, local_heads, -1) + projection_bias
    block_start = lax.axis_index("fsdp") * block_rows
    positions = block_start + jnp.arange(block_rows, dtype=jnp.int32)
    document_position = positions - doc_start
    query_rows = apply_rotation(
        projected_rows[..., : QUERY_PER_KV * HEAD_SIZE].reshape(
            block_rows, local_heads, QUERY_PER_KV, HEAD_SIZE
        ),
        document_position,
    ).astype(jnp.bfloat16)
    key_part = apply_rotation(
        projected_rows[..., QUERY_PER_KV * HEAD_SIZE : (QUERY_PER_KV + 1) * HEAD_SIZE],
        document_position,
    )
    keys_values = jnp.concatenate(
        [key_part, projected_rows[..., (QUERY_PER_KV + 1) * HEAD_SIZE :]], axis=-1
    ).astype(jnp.bfloat16)
    before = passed_along(keys_values[block_rows - KEYS_VISIBLE :], "fsdp", 1)
    head_rows = min(KEYS_VISIBLE, block_rows)
    body_rows = (block_rows - head_rows) // 2

    def one_query_block(first_row, query_count, key_rows):
        key_pos = (
            block_start
            - KEYS_VISIBLE
            + first_row
            + jnp.arange(query_count + KEYS_VISIBLE, dtype=jnp.int32)
        )
        return attend_block(
            query_rows[first_row : first_row + query_count],
            key_rows,
            positions[first_row : first_row + query_count],
            key_pos,
            doc_start[first_row : first_row + query_count],
            sinks,
        )

    later = [
        one_query_block(
            first_row,
            query_count,
            keys_values[first_row - KEYS_VISIBLE : first_row + query_count],
        )
        for first_row, query_count in (
            (head_rows, body_rows),
            (head_rows + body_rows, block_rows - head_rows - body_rows),
        )
    ]
    before, later = lax.optimization_barrier((before, later))
    extended = jnp.concatenate([before, keys_values[:head_rows]], axis=0)
    outputs_list = [one_query_block(0, head_rows, extended)] + later
    attention_result = jnp.concatenate(outputs_list, axis=0).reshape(block_rows, -1)
    out_full, attention_result = lax.optimization_barrier((out_full, attention_result))
    output_weights = out_full.reshape(-1, model_width)
    projection_step = with_layout_constraint(
        jnp.dot(attention_result, output_weights, preferred_element_type=jnp.float32).astype(
            jnp.bfloat16
        ),
        Layout((0, 1)),
    )
    projection_step = lax.psum_scatter(
        projection_step,
        ("ey", "ec"),
        scatter_dimension=0,
        tiled=True,
    ).astype(jnp.float32)
    return (widened + projection_step + b_out).astype(jnp.bfloat16)


def solution(mesh):
    n_fsdp, n_expert = mesh.devices.shape
    split_mesh = Mesh(mesh.devices.reshape(n_fsdp, n_expert // 2, 2), ("fsdp", "ey", "ec"))
    expert = ("ey", "ec")
    in_specs = (
        P("fsdp", expert, None, None, None),
        P(("fsdp",) + expert, None),
        P(("fsdp",) + expert, None),
        P(("fsdp",) + expert, None),
        P(("fsdp",) + expert, None),
        P("fsdp"),
        P(),
        P("fsdp", expert, None),
        P(expert, None),
        P(expert, None),
        P(expert, "fsdp", None),
        P(),
    )
    out_specs = P(("fsdp",) + expert, None)
    return jax.shard_map(shards, mesh=split_mesh, in_specs=in_specs, out_specs=out_specs, check_vma=False)
```

```python
import jax
import jax.numpy as jnp
from jax import lax
from jax.experimental.layout import Layout, with_layout_constraint
from jax.sharding import PartitionSpec as P

HEAD_SIZE = 64
QUERY_PER_KV = 8
TOPK = 4
KEYS_VISIBLE = 128


ROPE_BASE = 150000.0
EPSILON = 1e-05


def passed_along(block, axis, distance):
    devices = range(lax.axis_size(axis))
    route = [(i - distance, i) for i in devices if i - distance in devices]
    return lax.ppermute(block, axis, route)


def apply_rotation(values, positions):
    half_width = values.shape[-1] // 2
    steps_half = jnp.arange(half_width, dtype=jnp.float32)
    frequency = ROPE_BASE ** (-2.0 * steps_half / values.shape[-1])
    angles = positions.astype(jnp.float32)[:, None] * frequency[None, :]
    shape_out = (angles.shape[0],) + (1,) * (values.ndim - 2) + (half_width,)
    cosine = jnp.cos(angles).reshape(shape_out)
    sine_part = jnp.sin(angles).reshape(shape_out)
    front_half = values[..., :half_width]
    back_half = values[..., half_width:]
    return jnp.concatenate(
        [front_half * cosine - back_half * sine_part, back_half * cosine + front_half * sine_part],
        axis=-1,
    )


def attend_block(query_rows, key_rows, query_pos, key_pos, starts, sinks):
    keys_only = key_rows[..., :HEAD_SIZE]
    values_only = key_rows[..., HEAD_SIZE:]
    scores = jnp.einsum(
        "qjgd,kjd->jgqk", query_rows, keys_only, preferred_element_type=jnp.float32
    ) * HEAD_SIZE ** (-0.5)
    allowed = (
        (key_pos[None, :] <= query_pos[:, None])
        & (key_pos[None, :] > query_pos[:, None] - KEYS_VISIBLE)
        & (key_pos[None, :] >= starts[:, None])
    )
    masked = jnp.where(allowed[None, None], scores, -jnp.inf)
    row_peak = jnp.maximum(jnp.max(masked, axis=-1), sinks[:, :, None])
    exponent = jnp.exp(masked - row_peak[..., None])
    denominator = jnp.sum(exponent, axis=-1) + jnp.exp(sinks[:, :, None] - row_peak)
    weights_soft = (exponent / denominator[..., None]).astype(jnp.bfloat16)
    return jnp.einsum(
        "jgqk,kjd->qjgd", weights_soft, values_only, preferred_element_type=jnp.float32
    ).astype(jnp.bfloat16)


def gather_fsdp(block):
    count = lax.axis_size("fsdp")
    spread = jnp.broadcast_to(block[None], (count,) + block.shape)
    return lax.all_to_all(spread, "fsdp", split_axis=0, concat_axis=0, tiled=True)


def shards(
    expert_rows,
    residual,
    route_ids,
    route_weights,
    route_slots,
    doc_start,
    norm_gain,
    projection_weight,
    projection_bias,
    sinks,
    output_weight,
    b_out,
):
    own_rows = residual.shape[0]
    model_width = residual.shape[1]
    returned = lax.all_to_all(expert_rows, "expert", split_axis=2, concat_axis=1, tiled=True)
    qkv_full = lax.all_gather(projection_weight, "fsdp", axis=0, tiled=True)
    qkv_full, returned = lax.optimization_barrier((qkv_full, returned))
    all_experts = returned.shape[1]
    capacity = returned.shape[3]
    hit_expert = route_ids[..., None] == jnp.arange(all_experts, dtype=jnp.int32)
    hit_slot = route_slots[..., None] == jnp.arange(capacity, dtype=jnp.int32)
    hits = hit_expert[..., :, None] & hit_slot[..., None, :]
    select = jnp.sum(jnp.where(hits, route_weights[..., None, None], 0.0), axis=1)
    combined = jnp.einsum(
        "txs,xsm->tm",
        select.astype(jnp.bfloat16),
        returned[0, :, 0],
        preferred_element_type=jnp.float32,
    )
    hidden = (residual.astype(jnp.float32) + combined).astype(jnp.bfloat16)
    widened = hidden.astype(jnp.float32)
    normalized_rows = (
        widened
        * lax.rsqrt(jnp.mean(widened * widened, axis=-1, keepdims=True) + EPSILON)
        * norm_gain
    ).astype(jnp.bfloat16)
    gathered = lax.all_gather(normalized_rows, "expert", axis=0, tiled=True)
    out_full = gather_fsdp(output_weight[0])
    block_rows = gathered.shape[0]
    local_heads = projection_weight.shape[1]
    projected_rows = jnp.dot(
        gathered, qkv_full.reshape(model_width, -1), preferred_element_type=jnp.float32
    )
    projected_rows = projected_rows.reshape(block_rows, local_heads, -1) + projection_bias
    block_start = lax.axis_index("fsdp") * block_rows
    positions = block_start + jnp.arange(block_rows, dtype=jnp.int32)
    document_position = positions - doc_start
    query_rows = apply_rotation(
        projected_rows[..., : QUERY_PER_KV * HEAD_SIZE].reshape(
            block_rows, local_heads, QUERY_PER_KV, HEAD_SIZE
        ),
        document_position,
    ).astype(jnp.bfloat16)
    key_part = apply_rotation(
        projected_rows[..., QUERY_PER_KV * HEAD_SIZE : (QUERY_PER_KV + 1) * HEAD_SIZE],
        document_position,
    )
    keys_values = jnp.concatenate(
        [key_part, projected_rows[..., (QUERY_PER_KV + 1) * HEAD_SIZE :]], axis=-1
    ).astype(jnp.bfloat16)
    before = passed_along(keys_values[block_rows - KEYS_VISIBLE :], "fsdp", 1)
    head_rows = min(KEYS_VISIBLE, block_rows)
    body_rows = (block_rows - head_rows) // 2

    def one_query_block(first_row, query_count, key_rows):
        key_pos = (
            block_start
            - KEYS_VISIBLE
            + first_row
            + jnp.arange(query_count + KEYS_VISIBLE, dtype=jnp.int32)
        )
        return attend_block(
            query_rows[first_row : first_row + query_count],
            key_rows,
            positions[first_row : first_row + query_count],
            key_pos,
            doc_start[first_row : first_row + query_count],
            sinks,
        )

    later = [
        one_query_block(
            first_row,
            query_count,
            keys_values[first_row - KEYS_VISIBLE : first_row + query_count],
        )
        for first_row, query_count in (
            (head_rows, body_rows),
            (head_rows + body_rows, block_rows - head_rows - body_rows),
        )
    ]
    before, later = lax.optimization_barrier((before, later))
    extended = jnp.concatenate([before, keys_values[:head_rows]], axis=0)
    outputs_list = [one_query_block(0, head_rows, extended)] + later
    attention_result = jnp.concatenate(outputs_list, axis=0).reshape(block_rows, -1)
    out_full, attention_result = lax.optimization_barrier((out_full, attention_result))
    output_weights = out_full.reshape(-1, model_width)
    projection_step = with_layout_constraint(
        jnp.dot(attention_result, output_weights, preferred_element_type=jnp.float32).astype(
            jnp.bfloat16
        ),
        Layout((0, 1)),
    )
    projection_step = lax.psum_scatter(
        projection_step,
        "expert",
        scatter_dimension=0,
        tiled=True,
    ).astype(jnp.float32)
    return (widened + projection_step + b_out).astype(jnp.bfloat16)


def solution(mesh):
    in_specs = (
        P("fsdp", "expert", None, None, None),
        P(("fsdp", "expert"), None),
        P(("fsdp", "expert"), None),
        P(("fsdp", "expert"), None),
        P(("fsdp", "expert"), None),
        P("fsdp"),
        P(),
        P("fsdp", "expert", None),
        P("expert", None),
        P("expert", None),
        P("expert", "fsdp", None),
        P(),
    )
    out_specs = P(("fsdp", "expert"), None)
    return jax.shard_map(shards, mesh=mesh, in_specs=in_specs, out_specs=out_specs, check_vma=False)
```
